512 devices in a mesh: seq: 16 (over y, x_lo), chan: 32 (over z, x_hi, core).
Axes of the slice: x: 4 (x_hi: 2, x_lo: 2; x = x_hi * 2 + x_lo), y: 8, z: 8, core: 2. Of those that a mesh axis runs over, the one named last changes fastest.
Arguments:
- stream_in: bfloat16 [2048, 8192], P('seq', 'chan'), may hold values from -64 to 64
- outer_gate: bfloat16 [2048, 8192], P('seq', 'chan'), may hold values from -4 to 4
- inner_gate: bfloat16 [2048, 8192], P('seq', 'chan'), may hold values from -4 to 4
- values: bfloat16 [2048, 8192], P('seq', 'chan'), may hold values from -4 to 4
- long_filter: bfloat16 [2048, 8192], P('seq', 'chan'), may hold values from -1.2 to 1.2
- norm_gain: float32 [8192], P('chan'), may hold values from 0.5 to 1.5
- cotangent: bfloat16 [2048, 8192], P('seq', 'chan'), may hold values from -16 to 16
Outputs:
- normed: bfloat16 [2048, 8192], P('seq', 'chan')
- stream_grad: bfloat16 [2048, 8192], P('seq', 'chan')
- outer_grad: bfloat16 [2048, 8192], P('seq', 'chan')
- inner_grad: bfloat16 [2048, 8192], P('seq', 'chan')
- value_grad: bfloat16 [2048, 8192], P('seq', 'chan')
The draws below stay inside these ranges and needn't reach their ends.
All inputs are finite; a program needn't handle non-finite values.
Results may differ from the reference program's by a relative error of at most 0.012.
Values may be sent and summed in bfloat16 or wider, within the bound.
No kernel may reach another device: no remote copies, remote signals or barrier semaphores. Data moves between devices by JAX's collectives and lax.ppermute only.
A program may use at most 64 MiB of HBM per device.

```python
import jax
import jax.numpy as jnp
from jax import lax

MODEL_WIDTH = 8192
TOK_DEV = 128
BLOCKS = 16
TOKEN_COUNT = 2048


def common_parts(key):
    base_key = jax.random.fold_in(key, 101)
    base = jnp.clip(jax.random.normal(base_key, (TOKEN_COUNT, MODEL_WIDTH), jnp.float32), -4.0, 4.0)
    lower_end = 0.4
    upper_end = 4.0
    column = lower_end * (upper_end / lower_end) ** (jnp.arange(MODEL_WIDTH, dtype=jnp.float32) / (MODEL_WIDTH - 1))
    return (base, column, lower_end, upper_end)


def draw_stream_in(key, part):
    base, column, lower_end, upper_end = common_parts(key)
    row_scale = jnp.exp(jax.random.uniform(jax.random.fold_in(key, 202), (TOKEN_COUNT, 1), jnp.float32, jnp.log(lower_end), jnp.log(upper_end)))
    return (base * column * row_scale).astype(jnp.bfloat16)


def draw_cotangent(key, part):
    base, column, lower_end, upper_end = common_parts(key)
    noise_key = jax.random.fold_in(key, 303)
    noise = jnp.clip(jax.random.normal(noise_key, (TOKEN_COUNT, MODEL_WIDTH), jnp.float32), -4.0, 4.0)
    return (0.5 * base * column + noise).astype(jnp.bfloat16)


def draw_long_filter(key, part):
    random_keys = jax.random.split(key, 4)
    token_position = jnp.arange(TOKEN_COUNT, dtype=jnp.float32)[:, None]
    shortest = 24.0
    noise = jnp.clip(jax.random.normal(random_keys[3], (TOKEN_COUNT, MODEL_WIDTH), jnp.float32), -5.0, 5.0)
    longest = 40.0 * TOKEN_COUNT
    decay_len = jnp.exp(jax.random.uniform(random_keys[0], (MODEL_WIDTH,), jnp.float32, jnp.log(shortest), jnp.log(longest)))
    amplitude = 0.8 * jnp.sqrt(2.0 / jnp.minimum(decay_len, float(TOKEN_COUNT)))
    pulse_location = jax.random.randint(random_keys[1], (4, MODEL_WIDTH), 0, TOKEN_COUNT).astype(jnp.float32)
    pulse_retained = jax.random.uniform(random_keys[2], (4, MODEL_WIDTH), jnp.float32, 0.5, 0.8)
    decay_profile = jnp.exp(-token_position / decay_len)
    for pulse_index in range(4):
        decay_profile = decay_profile * jnp.where(token_position >= pulse_location[pulse_index], pulse_retained[pulse_index], 1.0)
    return (amplitude * decay_profile * noise).astype(jnp.bfloat16)


def block_levels(stream_key, dims, cuts, low, high):
    loudness = 1.0
    for dim, shards_of in cuts:
        draws = jax.random.uniform(jax.random.fold_in(jax.random.fold_in(stream_key, 6), dim), (shards_of,), jnp.float32, low / len(cuts), high / len(cuts))
        loudness = loudness * jnp.repeat(jnp.exp(draws), dims[dim] // shards_of).reshape((-1,) + (1,) * (len(dims) - 1 - dim))
    return loudness


def bell_draw(key, extent, width, bound, cuts=(), kind=jnp.bfloat16):
    array = width * jax.random.normal(key, extent, jnp.float32)
    if cuts:
        array = array * block_levels(key, extent, cuts, -0.22, 0.18)
    return jnp.clip(array, -bound, bound).astype(kind)


def setup_inputs(seed: int = 0) -> dict:
    keys = jax.random.split(jax.random.key(seed), 8)
    return {
        "stream_in": draw_stream_in(jax.random.fold_in(keys[7], 71), 0),
        "outer_gate": bell_draw(keys[1], (TOKEN_COUNT, MODEL_WIDTH), 1.0, 4.0, ((0, 16), (1, 32))),
        "inner_gate": bell_draw(keys[2], (TOKEN_COUNT, MODEL_WIDTH), 1.0, 4.0, ((0, 16), (1, 32))),
        "values": bell_draw(keys[3], (TOKEN_COUNT, MODEL_WIDTH), 1.0, 4.0, ((0, 16), (1, 32))),
        "long_filter": draw_long_filter(jax.random.fold_in(keys[7], 71), 0),
        "norm_gain": jnp.clip(1.0 + 0.1 * jax.random.normal(keys[5], (MODEL_WIDTH,), jnp.float32), 0.5, 1.5),
        "cotangent": draw_cotangent(jax.random.fold_in(keys[7], 71), 0),
    }


def packed_spectrum(columns):
    half = columns.shape[1] // 2
    spectrum = jnp.fft.rfft(columns, axis=1)
    return jnp.concatenate([spectrum.real[:, :half], spectrum.real[:, half:half + 1], spectrum.imag[:, 1:half]], axis=1)

def from_spectrum(packed):
    half = packed.shape[1] // 2
    real_part = packed[:, :half + 1]
    zero_row = jnp.zeros_like(packed[:, :1])
    imag_part = jnp.concatenate([zero_row, packed[:, half + 1:], zero_row], axis=1)
    return jnp.fft.irfft(lax.complex(real_part, imag_part), n=2 * half, axis=1)

def spectral_product(left, right, conjugate):
    half = left.shape[-2] // 2
    left_real, left_imag = (left[..., :half, :], left[..., half:, :])
    right_real, right_imag = (right[..., :half, :], right[..., half:, :])
    first_bin = lax.broadcasted_iota(jnp.int32, (half, 1), 0) == 0
    if conjugate:
        right_eff = jnp.where(first_bin, right_imag, -right_imag)
    else:
        right_eff = right_imag
    real_out = left_real * right_real - jnp.where(first_bin, 0.0, left_imag * right_eff)
    imag_out = jnp.where(first_bin, left_imag * right_imag, left_real * right_eff + left_imag * right_real)
    return jnp.concatenate([real_out, imag_out], axis=-2)

def rounded(values_in):
    narrow = values_in.astype(jnp.bfloat16)
    return lax.optimization_barrier(narrow).astype(jnp.float32)

def reference(stream_in, outer_gate, inner_gate, values, long_filter, norm_gain, cotangent):
    half = TOK_DEV
    blocks = BLOCKS
    outer = outer_gate.astype(jnp.float32)
    inner = inner_gate.astype(jnp.float32)
    value_rows = values.astype(jnp.float32)
    mixed = inner * value_rows
    zero_half = jnp.zeros((blocks, half, MODEL_WIDTH), jnp.float32)
    data_spec = rounded(packed_spectrum(jnp.concatenate([mixed.reshape(blocks, half, MODEL_WIDTH), zero_half], axis=1)))
    filt_rows = long_filter.astype(jnp.float32).reshape(blocks, half, MODEL_WIDTH)
    filt_spec = rounded(packed_spectrum(jnp.concatenate([filt_rows, zero_half], axis=1)))
    padded_data = jnp.concatenate([jnp.zeros_like(data_spec), data_spec], axis=0)

    def forward_lag(lag_index, running):
        lag = jnp.asarray(lag_index).astype(jnp.int32)
        start = (jnp.int32(blocks) - lag).astype(jnp.int32)
        shifted = lax.dynamic_slice_in_dim(padded_data, start, blocks, 0)
        taps = lax.dynamic_index_in_dim(filt_spec, lag, 0, keepdims=False)
        return running + spectral_product(shifted, taps, False)
    total = lax.fori_loop(0, blocks, forward_lag, jnp.zeros((blocks, 2 * half, MODEL_WIDTH), jnp.float32))
    waveform = from_spectrum(total)
    spill = jnp.concatenate([jnp.zeros((1, half, MODEL_WIDTH), jnp.float32), waveform[:-1, half:]], axis=0)
    conv = (waveform[:, :half] + spill).reshape(TOKEN_COUNT, MODEL_WIDTH)
    resid = stream_in.astype(jnp.float32) + outer * conv
    inv_rms = lax.rsqrt(lax.optimization_barrier(jnp.mean(resid * resid, axis=1, keepdims=True)) + 1e-06)
    normed = (resid * inv_rms * norm_gain).astype(jnp.bfloat16)
    scaled = cotangent.astype(jnp.float32) * norm_gain
    proj = lax.optimization_barrier(jnp.mean(scaled * resid, axis=1, keepdims=True))
    grad_resid = inv_rms * (scaled - resid * inv_rms * inv_rms * proj)
    outer_grad = (grad_resid * conv).astype(jnp.bfloat16)
    dconv = (grad_resid * outer).reshape(blocks, half, MODEL_WIDTH)
    following = jnp.concatenate([dconv[1:], jnp.zeros((1, half, MODEL_WIDTH), jnp.float32)], axis=0)
    back_spec = rounded(packed_spectrum(jnp.concatenate([dconv, following], axis=1)))
    padded_back = jnp.concatenate([back_spec, jnp.zeros_like(back_spec)], axis=0)

    def backward_lag(lag_index, running):
        lag = jnp.asarray(lag_index).astype(jnp.int32)
        shifted = lax.dynamic_slice_in_dim(padded_back, lag, blocks, 0)
        taps = lax.dynamic_index_in_dim(filt_spec, lag, 0, keepdims=False)
        return running + spectral_product(shifted, taps, True)
    back_total = lax.fori_loop(0, blocks, backward_lag, jnp.zeros((blocks, 2 * half, MODEL_WIDTH), jnp.float32))
    dmixed = from_spectrum(back_total)[:, :half].reshape(TOKEN_COUNT, MODEL_WIDTH)
    inner_grad = (dmixed * value_rows).astype(jnp.bfloat16)
    value_grad = (dmixed * inner).astype(jnp.bfloat16)
    return (normed, grad_resid.astype(jnp.bfloat16), outer_grad, inner_grad, value_grad)
```

```python
import math

import numpy as np

import jax
import jax.numpy as jnp
from jax import lax
from jax.sharding import PartitionSpec as P

EPSILON = 1e-06
HIGHEST_MODE = lax.Precision.HIGHEST


def dft_tables(half):
    length = 2 * half
    rows = np.arange(length)[:, None]
    cols = np.arange(length)[None, :]
    step = math.pi / half
    phase = (rows % half * cols % length).astype(np.float64) * step
    nyquist = (half * cols % length).astype(np.float64) * step
    forward = np.where(
        rows < half, np.cos(phase), np.where(rows == half, np.cos(nyquist), -np.sin(phase))
    )
    phase_back = (cols % half * rows % length).astype(np.float64) * step
    nyquist_back = (half * rows % length).astype(np.float64) * step
    weight = np.where(cols == 0, 1.0, 2.0)
    inverse = np.where(
        cols < half,
        weight * np.cos(phase_back),
        np.where(cols == half, np.cos(nyquist_back), -2.0 * np.sin(phase_back)),
    )
    return forward.astype(np.float32), (inverse / length).astype(np.float32)


def spectral_product(left, right, conjugate):
    half = left.shape[-1] // 2
    left_real, left_imag = (left[..., :half], left[..., half:])
    right_real, right_imag = (right[..., :half], right[..., half:])
    first_bin = lax.broadcasted_iota(jnp.int32, (1,) * (left.ndim - 1) + (half,), left.ndim - 1) == 0
    if conjugate:
        right_eff = jnp.where(first_bin, right_imag, -right_imag)
    else:
        right_eff = right_imag
    real_out = left_real * right_real - jnp.where(first_bin, 0.0, left_imag * right_eff)
    imag_out = jnp.where(
        first_bin, left_imag * right_imag, left_real * right_eff + left_imag * right_real
    )
    return jnp.concatenate([real_out, imag_out], axis=-1)


def rows_times(left, table):
    return lax.dot_general(
        left, table, (((left.ndim - 1,), (1,)), ((), ())),
        precision=HIGHEST_MODE, preferred_element_type=jnp.float32,
    )


def to_channels(x, parts):
    tok, width = x.shape[-2], x.shape[-1]
    lead = x.shape[:-2]
    xt = jnp.swapaxes(x, -1, -2).reshape(lead + (parts, width // parts, tok))
    xt = jnp.moveaxis(xt, len(lead), 0)
    return lax.all_to_all(xt, "seq", 0, 0)


def from_channels(xc):
    back = lax.all_to_all(xc, "seq", 0, 0)
    back = jnp.moveaxis(back, 0, -3)
    shape = back.shape
    back = back.reshape(shape[:-3] + (shape[-3] * shape[-2], shape[-1]))
    return jnp.swapaxes(back, -1, -2)


def body(stream_in, outer_gate, inner_gate, values, long_filter, norm_gain, cotangent):
    half = stream_in.shape[0]
    width = stream_in.shape[1]
    parts = lax.axis_size("seq")
    forward_np, inverse_np = dft_tables(half)
    forward = jnp.asarray(forward_np)
    forward_half = jnp.asarray(forward_np[:, :half])
    inverse = jnp.asarray(inverse_np)
    inverse_half = jnp.asarray(inverse_np[:half])

    stacked = jnp.stack([inner_gate, values, long_filter], axis=0)
    chan_in = to_channels(stacked, parts)
    inner_c = chan_in[:, 0].astype(jnp.float32)
    values_c = chan_in[:, 1].astype(jnp.float32)
    filt_c = chan_in[:, 2].astype(jnp.float32)
    blocks = chan_in.shape[0]

    mixed_c = inner_c * values_c
    data_spec = rows_times(mixed_c, forward_half)
    filt_spec = rows_times(filt_c, forward_half)

    total = spectral_product(data_spec, filt_spec[0][None], False)
    for lag in range(1, blocks):
        shifted = jnp.concatenate(
            [jnp.zeros((lag,) + data_spec.shape[1:], jnp.float32), data_spec[: blocks - lag]], axis=0
        )
        total = total + spectral_product(shifted, filt_spec[lag][None], False)
    waveform = rows_times(total, inverse)
    spill = jnp.concatenate(
        [jnp.zeros((1,) + waveform.shape[1:2] + (half,), jnp.float32), waveform[:-1, :, half:]], axis=0
    )
    conv_c = waveform[..., :half] + spill
    conv = from_channels(conv_c)

    outer = outer_gate.astype(jnp.float32)
    resid = stream_in.astype(jnp.float32) + outer * conv
    scaled = cotangent.astype(jnp.float32) * norm_gain
    square_sum, proj_sum = lax.psum(
        (
            jnp.sum(resid * resid, axis=1, keepdims=True),
            jnp.sum(scaled * resid, axis=1, keepdims=True),
        ),
        "chan",
    )
    total_width = width * lax.axis_size("chan")
    inv_rms = lax.rsqrt(square_sum / total_width + EPSILON)
    normed = (resid * inv_rms * norm_gain).astype(jnp.bfloat16)
    grad_resid = inv_rms * (scaled - resid * inv_rms * inv_rms * (proj_sum / total_width))
    outer_grad = (grad_resid * conv).astype(jnp.bfloat16)
    dconv = grad_resid * outer

    dconv_c = to_channels(dconv, parts)
    following = jnp.concatenate([dconv_c[1:], jnp.zeros_like(dconv_c[:1])], axis=0)
    back_spec = rows_times(jnp.concatenate([dconv_c, following], axis=-1), forward)
    back_total = spectral_product(back_spec, filt_spec[0][None], True)
    for lag in range(1, blocks):
        shifted = jnp.concatenate(
            [back_spec[lag:], jnp.zeros((lag,) + back_spec.shape[1:], jnp.float32)], axis=0
        )
        back_total = back_total + spectral_product(shifted, filt_spec[lag][None], True)
    dmixed_c = rows_times(back_total, inverse_half)
    grads_c = jnp.stack(
        [(dmixed_c * values_c).astype(jnp.bfloat16), (dmixed_c * inner_c).astype(jnp.bfloat16)],
        axis=1,
    )
    grads = from_channels(grads_c)
    return (normed, grad_resid.astype(jnp.bfloat16), outer_grad, grads[0], grads[1])


def solution(mesh):
    placed = (
        P("seq", "chan"),
        P("seq", "chan"),
        P("seq", "chan"),
        P("seq", "chan"),
        P("seq", "chan"),
        P("chan"),
        P("seq", "chan"),
    )
    return jax.shard_map(
        body,
        mesh=mesh,
        in_specs=placed,
        out_specs=(
            P("seq", "chan"),
            P("seq", "chan"),
            P("seq", "chan"),
            P("seq", "chan"),
            P("seq", "chan"),
        ),
        check_vma=False,
    )
```

```python
import math

import numpy as np

import jax
import jax.numpy as jnp
from jax import lax
from jax.sharding import PartitionSpec as P

EPSILON = 1e-06
HIGHEST_MODE = lax.Precision.HIGHEST


def dft_tables(half):
    length = 2 * half
    rows = np.arange(length)[:, None]
    cols = np.arange(length)[None, :]
    step = math.pi / half
    phase = (rows % half * cols % length).astype(np.float64) * step
    nyquist = (half * cols % length).astype(np.float64) * step
    forward = np.where(
        rows < half, np.cos(phase), np.where(rows == half, np.cos(nyquist), -np.sin(phase))
    )
    phase_back = (cols % half * rows % length).astype(np.float64) * step
    nyquist_back = (half * rows % length).astype(np.float64) * step
    weight = np.where(cols == 0, 1.0, 2.0)
    inverse = np.where(
        cols < half,
        weight * np.cos(phase_back),
        np.where(cols == half, np.cos(nyquist_back), -2.0 * np.sin(phase_back)),
    )
    return forward.astype(np.float32), (inverse / length).astype(np.float32)


def spectral_product(left, right, conjugate):
    half = left.shape[-1] // 2
    left_real, left_imag = (left[..., :half], left[..., half:])
    right_real, right_imag = (right[..., :half], right[..., half:])
    first_bin = lax.broadcasted_iota(jnp.int32, (1,) * (left.ndim - 1) + (half,), left.ndim - 1) == 0
    if conjugate:
        right_eff = jnp.where(first_bin, right_imag, -right_imag)
    else:
        right_eff = right_imag
    real_out = left_real * right_real - jnp.where(first_bin, 0.0, left_imag * right_eff)
    imag_out = jnp.where(
        first_bin, left_imag * right_imag, left_real * right_eff + left_imag * right_real
    )
    return jnp.concatenate([real_out, imag_out], axis=-1)


def rows_times(left, table):
    return lax.dot_general(
        left, table, (((left.ndim - 1,), (1,)), ((), ())),
        precision=HIGHEST_MODE, preferred_element_type=jnp.float32,
    )


def to_channels(x, parts):
    tok, width = x.shape[-2], x.shape[-1]
    lead = x.shape[:-2]
    xt = jnp.swapaxes(x, -1, -2).reshape(lead + (parts, width // parts, tok))
    xt = jnp.moveaxis(xt, len(lead), 0)
    return lax.all_to_all(xt, "seq", 0, 0)


def from_channels(xc):
    back = lax.all_to_all(xc, "seq", 0, 0)
    back = jnp.moveaxis(back, 0, -3)
    shape = back.shape
    back = back.reshape(shape[:-3] + (shape[-3] * shape[-2], shape[-1]))
    return jnp.swapaxes(back, -1, -2)


def chan_sum(partial):
    count = lax.axis_size("chan")
    spread = jnp.broadcast_to(partial[None], (count,) + partial.shape)
    return jnp.sum(lax.all_to_all(spread, "chan", 0, 0), axis=0)


def body(stream_in, outer_gate, inner_gate, values, long_filter, norm_gain, cotangent):
    half = stream_in.shape[0]
    width = stream_in.shape[1]
    parts = lax.axis_size("seq")
    forward_np, inverse_np = dft_tables(half)
    forward = jnp.asarray(forward_np)
    forward_half = jnp.asarray(forward_np[:, :half])
    inverse = jnp.asarray(inverse_np)
    inverse_half = jnp.asarray(inverse_np[:half])

    stacked = jnp.stack([inner_gate, values, long_filter], axis=0)
    chan_in = to_channels(stacked, parts)
    inner_c = chan_in[:, 0].astype(jnp.float32)
    values_c = chan_in[:, 1].astype(jnp.float32)
    filt_c = chan_in[:, 2].astype(jnp.float32)
    blocks = chan_in.shape[0]

    mixed_c = inner_c * values_c
    data_spec = rows_times(mixed_c, forward_half)
    filt_spec = rows_times(filt_c, forward_half)

    total = spectral_product(data_spec, filt_spec[0][None], False)
    for lag in range(1, blocks):
        shifted = jnp.concatenate(
            [jnp.zeros((lag,) + data_spec.shape[1:], jnp.float32), data_spec[: blocks - lag]], axis=0
        )
        total = total + spectral_product(shifted, filt_spec[lag][None], False)
    waveform = rows_times(total, inverse)
    spill = jnp.concatenate(
        [jnp.zeros((1,) + waveform.shape[1:2] + (half,), jnp.float32), waveform[:-1, :, half:]], axis=0
    )
    conv_c = waveform[..., :half] + spill
    conv = from_channels(conv_c)

    outer = outer_gate.astype(jnp.float32)
    resid = stream_in.astype(jnp.float32) + outer * conv
    scaled = cotangent.astype(jnp.float32) * norm_gain
    sums = chan_sum(
        jnp.concatenate(
            [
                jnp.sum(resid * resid, axis=1, keepdims=True),
                jnp.sum(scaled * resid, axis=1, keepdims=True),
            ],
            axis=1,
        )
    )
    square_sum, proj_sum = sums[:, 0:1], sums[:, 1:2]
    total_width = width * lax.axis_size("chan")
    inv_rms = lax.rsqrt(square_sum / total_width + EPSILON)
    normed = (resid * inv_rms * norm_gain).astype(jnp.bfloat16)
    grad_resid = inv_rms * (scaled - resid * inv_rms * inv_rms * (proj_sum / total_width))
    outer_grad = (grad_resid * conv).astype(jnp.bfloat16)
    dconv = grad_resid * outer

    dconv_c = to_channels(dconv, parts)
    following = jnp.concatenate([dconv_c[1:], jnp.zeros_like(dconv_c[:1])], axis=0)
    back_spec = rows_times(jnp.concatenate([dconv_c, following], axis=-1), forward)
    back_total = spectral_product(back_spec, filt_spec[0][None], True)
    for lag in range(1, blocks):
        shifted = jnp.concatenate(
            [back_spec[lag:], jnp.zeros((lag,) + back_spec.shape[1:], jnp.float32)], axis=0
        )
        back_total = back_total + spectral_product(shifted, filt_spec[lag][None], True)
    dmixed_c = rows_times(back_total, inverse_half)
    grads_c = jnp.stack(
        [(dmixed_c * values_c).astype(jnp.bfloat16), (dmixed_c * inner_c).astype(jnp.bfloat16)],
        axis=1,
    )
    grads = from_channels(grads_c)
    return (normed, grad_resid.astype(jnp.bfloat16), outer_grad, grads[0], grads[1])


def solution(mesh):
    placed = (
        P("seq", "chan"),
        P("seq", "chan"),
        P("seq", "chan"),
        P("seq", "chan"),
        P("seq", "chan"),
        P("chan"),
        P("seq", "chan"),
    )
    return jax.shard_map(
        body,
        mesh=mesh,
        in_specs=placed,
        out_specs=(
            P("seq", "chan"),
            P("seq", "chan"),
            P("seq", "chan"),
            P("seq", "chan"),
            P("seq", "chan"),
        ),
        check_vma=False,
    )
```

```python
import math

import numpy as np

import jax
import jax.numpy as jnp
from jax import lax
from jax.sharding import PartitionSpec as P

EPSILON = 1e-06
HIGHEST_MODE = lax.Precision.HIGHEST


def dft_tables(half):
    length = 2 * half
    rows = np.arange(length)[:, None]
    cols = np.arange(length)[None, :]
    step = math.pi / half
    phase = (rows % half * cols % length).astype(np.float64) * step
    nyquist = (half * cols % length).astype(np.float64) * step
    forward = np.where(
        rows < half, np.cos(phase), np.where(rows == half, np.cos(nyquist), -np.sin(phase))
    )
    phase_back = (cols % half * rows % length).astype(np.float64) * step
    nyquist_back = (half * rows % length).astype(np.float64) * step
    weight = np.where(cols == 0, 1.0, 2.0)
    inverse = np.where(
        cols < half,
        weight * np.cos(phase_back),
        np.where(cols == half, np.cos(nyquist_back), -2.0 * np.sin(phase_back)),
    )
    return forward.astype(np.float32), (inverse / length).astype(np.float32)


def spectral_product(left, right, conjugate):
    half = left.shape[-1] // 2
    left_real, left_imag = (left[..., :half], left[..., half:])
    right_real, right_imag = (right[..., :half], right[..., half:])
    first_bin = lax.broadcasted_iota(jnp.int32, (1,) * (left.ndim - 1) + (half,), left.ndim - 1) == 0
    if conjugate:
        right_eff = jnp.where(first_bin, right_imag, -right_imag)
    else:
        right_eff = right_imag
    real_out = left_real * right_real - jnp.where(first_bin, 0.0, left_imag * right_eff)
    imag_out = jnp.where(
        first_bin, left_imag * right_imag, left_real * right_eff + left_imag * right_real
    )
    return jnp.concatenate([real_out, imag_out], axis=-1)


def rows_times(left, table):
    return lax.dot_general(
        left, table, (((left.ndim - 1,), (1,)), ((), ())),
        precision=HIGHEST_MODE, preferred_element_type=jnp.float32,
    )


def to_channels(x, parts):
    tok, width = x.shape[-2], x.shape[-1]
    lead = x.shape[:-2]
    xt = jnp.swapaxes(x, -1, -2).reshape(lead + (parts, width // parts, tok))
    xt = jnp.moveaxis(xt, len(lead), 0)
    return lax.all_to_all(xt, "seq", 0, 0)


def from_channels(xc):
    back = lax.all_to_all(xc, "seq", 0, 0)
    back = jnp.moveaxis(back, 0, -3)
    shape = back.shape
    back = back.reshape(shape[:-3] + (shape[-3] * shape[-2], shape[-1]))
    return jnp.swapaxes(back, -1, -2)


def chan_sum(partial):
    count = lax.axis_size("chan")
    spread = jnp.broadcast_to(partial[None], (count,) + partial.shape)
    return jnp.sum(lax.all_to_all(spread, "chan", 0, 0), axis=0)


def body(stream_in, outer_gate, inner_gate, values, long_filter, norm_gain, cotangent):
    half = stream_in.shape[0]
    width = stream_in.shape[1]
    parts = lax.axis_size("seq")
    forward_np, inverse_np = dft_tables(half)
    forward = jnp.asarray(forward_np)
    forward_half = jnp.asarray(forward_np[:, :half])
    inverse = jnp.asarray(inverse_np)
    inverse_half = jnp.asarray(inverse_np[:half])

    stacked = jnp.stack([inner_gate, values, long_filter], axis=0)
    chan_in = to_channels(stacked, parts)
    inner_c = chan_in[:, 0].astype(jnp.float32)
    values_c = chan_in[:, 1].astype(jnp.float32)
    filt_c = chan_in[:, 2].astype(jnp.float32)
    blocks = chan_in.shape[0]

    mixed_c = inner_c * values_c
    data_spec = rows_times(mixed_c, forward_half)
    filt_spec = rows_times(filt_c, forward_half)

    total = spectral_product(data_spec, filt_spec[0][None], False)
    for lag in range(1, blocks):
        shifted = jnp.concatenate(
            [jnp.zeros((lag,) + data_spec.shape[1:], jnp.float32), data_spec[: blocks - lag]], axis=0
        )
        total = total + spectral_product(shifted, filt_spec[lag][None], False)
    waveform = rows_times(total, inverse)
    spill = jnp.concatenate(
        [jnp.zeros((1,) + waveform.shape[1:2] + (half,), jnp.float32), waveform[:-1, :, half:]], axis=0
    )
    conv_c = waveform[..., :half] + spill
    conv = from_channels(conv_c.astype(jnp.bfloat16)).astype(jnp.float32)

    outer = outer_gate.astype(jnp.float32)
    resid = stream_in.astype(jnp.float32) + outer * conv
    scaled = cotangent.astype(jnp.float32) * norm_gain
    sums = chan_sum(
        jnp.concatenate(
            [
                jnp.sum(resid * resid, axis=1, keepdims=True),
                jnp.sum(scaled * resid, axis=1, keepdims=True),
            ],
            axis=1,
        )
    )
    square_sum, proj_sum = sums[:, 0:1], sums[:, 1:2]
    total_width = width * lax.axis_size("chan")
    inv_rms = lax.rsqrt(square_sum / total_width + EPSILON)
    normed = (resid * inv_rms * norm_gain).astype(jnp.bfloat16)
    grad_resid = inv_rms * (scaled - resid * inv_rms * inv_rms * (proj_sum / total_width))
    outer_grad = (grad_resid * conv).astype(jnp.bfloat16)
    dconv = grad_resid * outer

    dconv_c = to_channels(dconv.astype(jnp.bfloat16), parts).astype(jnp.float32)
    following = jnp.concatenate([dconv_c[1:], jnp.zeros_like(dconv_c[:1])], axis=0)
    back_spec = rows_times(jnp.concatenate([dconv_c, following], axis=-1), forward)
    back_total = spectral_product(back_spec, filt_spec[0][None], True)
    for lag in range(1, blocks):
        shifted = jnp.concatenate(
            [back_spec[lag:], jnp.zeros((lag,) + back_spec.shape[1:], jnp.float32)], axis=0
        )
        back_total = back_total + spectral_product(shifted, filt_spec[lag][None], True)
    dmixed_c = rows_times(back_total, inverse_half)
    grads_c = jnp.stack(
        [(dmixed_c * values_c).astype(jnp.bfloat16), (dmixed_c * inner_c).astype(jnp.bfloat16)],
        axis=1,
    )
    grads = from_channels(grads_c)
    return (normed, grad_resid.astype(jnp.bfloat16), outer_grad, grads[0], grads[1])


def solution(mesh):
    placed = (
        P("seq", "chan"),
        P("seq", "chan"),
        P("seq", "chan"),
        P("seq", "chan"),
        P("seq", "chan"),
        P("chan"),
        P("seq", "chan"),
    )
    return jax.shard_map(
        body,
        mesh=mesh,
        in_specs=placed,
        out_specs=(
            P("seq", "chan"),
            P("seq", "chan"),
            P("seq", "chan"),
            P("seq", "chan"),
            P("seq", "chan"),
        ),
        check_vma=False,
    )
```

```python
import math

import numpy as np

import jax
import jax.numpy as jnp
from jax import lax
from jax.experimental import pallas as pl
from jax.experimental.pallas import tpu as pltpu
from jax.sharding import PartitionSpec as P

EPSILON = 1e-06
HIGHEST_MODE = lax.Precision.HIGHEST


def dft_tables(half):
    length = 2 * half
    rows = np.arange(length)[:, None]
    cols = np.arange(length)[None, :]
    step = math.pi / half
    phase = (rows % half * cols % length).astype(np.float64) * step
    nyquist = (half * cols % length).astype(np.float64) * step
    forward = np.where(
        rows < half, np.cos(phase), np.where(rows == half, np.cos(nyquist), -np.sin(phase))
    )
    phase_back = (cols % half * rows % length).astype(np.float64) * step
    nyquist_back = (half * rows % length).astype(np.float64) * step
    weight = np.where(cols == 0, 1.0, 2.0)
    inverse = np.where(
        cols < half,
        weight * np.cos(phase_back),
        np.where(cols == half, np.cos(nyquist_back), -2.0 * np.sin(phase_back)),
    )
    return forward.astype(np.float32), (inverse / length).astype(np.float32)


def spectral_product(left, right, conjugate):
    half = left.shape[-1] // 2
    left_real, left_imag = (left[..., :half], left[..., half:])
    right_real, right_imag = (right[..., :half], right[..., half:])
    first_bin = lax.broadcasted_iota(jnp.int32, (1,) * (left.ndim - 1) + (half,), left.ndim - 1) == 0
    if conjugate:
        right_eff = jnp.where(first_bin, right_imag, -right_imag)
    else:
        right_eff = right_imag
    real_out = left_real * right_real - jnp.where(first_bin, 0.0, left_imag * right_eff)
    imag_out = jnp.where(
        first_bin, left_imag * right_imag, left_real * right_eff + left_imag * right_real
    )
    return jnp.concatenate([real_out, imag_out], axis=-1)


def rows_times(left, table):
    return lax.dot_general(
        left, table, (((left.ndim - 1,), (1,)), ((), ())),
        precision=HIGHEST_MODE, preferred_element_type=jnp.float32,
    )


def packed_product(left, right, conjugate):
    half = left.shape[-1] // 2
    left_real, left_imag = (left[:, :half], left[:, half:])
    right_real, right_imag = (right[:, :half], right[:, half:])
    first_bin = lax.broadcasted_iota(jnp.int32, left_real.shape, 1) == 0
    if conjugate:
        right_eff = jnp.where(first_bin, right_imag, -right_imag)
    else:
        right_eff = right_imag
    real_out = left_real * right_real - jnp.where(first_bin, 0.0, left_imag * right_eff)
    imag_out = jnp.where(
        first_bin, left_imag * right_imag, left_real * right_eff + left_imag * right_real
    )
    return real_out, imag_out


def kdot(left, right):
    return jnp.dot(left, right, precision=HIGHEST_MODE, preferred_element_type=jnp.float32)


def tiled_rows(part, count):
    rows, lanes = part.shape
    return jnp.broadcast_to(part[None], (count, rows, lanes)).reshape(count * rows, lanes)


def forward_kernel(x_ref, fwd_ref, inv_ref, conv_ref, filt_ref, acc_ref):
    blocks, _, chans, tok = x_ref.shape
    rows = blocks * chans
    inner = x_ref[:, 0, :, :].astype(jnp.float32).reshape(rows, tok)
    value_rows = x_ref[:, 1, :, :].astype(jnp.float32).reshape(rows, tok)
    taps = x_ref[:, 2, :, :].astype(jnp.float32).reshape(rows, tok)
    table = fwd_ref[...]
    data_spec = kdot(inner * value_rows, table)
    filt_spec = kdot(taps, table)
    filt_ref[...] = filt_spec
    half = data_spec.shape[1] // 2
    real0, imag0 = packed_product(data_spec, tiled_rows(filt_spec[0:chans], blocks), False)
    acc_ref[:, :half] = real0
    acc_ref[:, half:] = imag0
    for lag in range(1, blocks):
        count = blocks - lag
        real, imag = packed_product(
            data_spec[: count * chans], tiled_rows(filt_spec[lag * chans : (lag + 1) * chans], count), False
        )
        acc_ref[lag * chans :, :half] += real
        acc_ref[lag * chans :, half:] += imag
    waveform = kdot(acc_ref[...], inv_ref[...])
    conv_ref[0:chans, :] = waveform[0:chans, :tok].astype(conv_ref.dtype)
    conv_ref[chans:, :] = (waveform[chans:, :tok] + waveform[: rows - chans, tok:]).astype(conv_ref.dtype)


def backward_kernel(d_ref, filt_ref, x_ref, fwd_ref, inv_ref, out_ref, fol_ref, acc_ref):
    blocks, _, chans, tok = x_ref.shape
    rows = blocks * chans
    dconv = d_ref[...].astype(jnp.float32)
    fol_ref[: rows - chans, :] = dconv[chans:, :]
    fol_ref[rows - chans :, :] = jnp.zeros((chans, tok), jnp.float32)
    back_spec = kdot(dconv, fwd_ref[:tok, :]) + kdot(fol_ref[...], fwd_ref[tok:, :])
    filt_spec = filt_ref[...]
    half = back_spec.shape[1] // 2
    real0, imag0 = packed_product(back_spec, tiled_rows(filt_spec[0:chans], blocks), True)
    acc_ref[:, :half] = real0
    acc_ref[:, half:] = imag0
    for lag in range(1, blocks):
        count = blocks - lag
        real, imag = packed_product(
            back_spec[lag * chans :], tiled_rows(filt_spec[lag * chans : (lag + 1) * chans], count), True
        )
        acc_ref[: count * chans, :half] += real
        acc_ref[: count * chans, half:] += imag
    dmixed = kdot(acc_ref[...], inv_ref[...]).reshape(blocks, chans, tok)
    inner = x_ref[:, 0, :, :].astype(jnp.float32)
    value_rows = x_ref[:, 1, :, :].astype(jnp.float32)
    out_ref[:, 0, :, :] = (dmixed * value_rows).astype(out_ref.dtype)
    out_ref[:, 1, :, :] = (dmixed * inner).astype(out_ref.dtype)


def vmem_call(kernel, outs, scratch, *args):
    return pl.pallas_call(
        kernel,
        out_shape=outs,
        in_specs=[pl.BlockSpec(memory_space=pltpu.VMEM) for _ in args],
        out_specs=tuple(pl.BlockSpec(memory_space=pltpu.VMEM) for _ in outs),
        scratch_shapes=scratch,
    )(*args)


def to_channels(x, parts):
    tok, width = x.shape[-2], x.shape[-1]
    lead = x.shape[:-2]
    xt = jnp.swapaxes(x, -1, -2).reshape(lead + (parts, width // parts, tok))
    xt = jnp.moveaxis(xt, len(lead), 0)
    return lax.all_to_all(xt, "seq", 0, 0)


def from_channels(xc):
    back = lax.all_to_all(xc, "seq", 0, 0)
    back = jnp.moveaxis(back, 0, -3)
    shape = back.shape
    back = back.reshape(shape[:-3] + (shape[-3] * shape[-2], shape[-1]))
    return jnp.swapaxes(back, -1, -2)


def chan_sum(partial):
    count = lax.axis_size("chan")
    spread = jnp.broadcast_to(partial[None], (count,) + partial.shape)
    return jnp.sum(lax.all_to_all(spread, "chan", 0, 0), axis=0)


def body(stream_in, outer_gate, inner_gate, values, long_filter, norm_gain, cotangent):
    half = stream_in.shape[0]
    width = stream_in.shape[1]
    parts = lax.axis_size("seq")
    forward_np, inverse_np = dft_tables(half)

    stacked = jnp.stack([inner_gate, values, long_filter], axis=0)
    chan_in = to_channels(stacked, parts)
    blocks, _, chans, tok = chan_in.shape
    rows = blocks * chans
    conv_c, filt_spec = vmem_call(
        forward_kernel,
        (
            jax.ShapeDtypeStruct((rows, tok), jnp.bfloat16),
            jax.ShapeDtypeStruct((rows, 2 * half), jnp.float32),
        ),
        [pltpu.VMEM((rows, 2 * half), jnp.float32)],
        chan_in, jnp.asarray(forward_np[:, :half].T), jnp.asarray(inverse_np.T),
    )
    conv_c = conv_c.reshape(blocks, chans, tok)
    conv = from_channels(conv_c).astype(jnp.float32)

    outer = outer_gate.astype(jnp.float32)
    resid = stream_in.astype(jnp.float32) + outer * conv
    scaled = cotangent.astype(jnp.float32) * norm_gain
    sums = chan_sum(
        jnp.concatenate(
            [
                jnp.sum(resid * resid, axis=1, keepdims=True),
                jnp.sum(scaled * resid, axis=1, keepdims=True),
            ],
            axis=1,
        )
    )
    square_sum, proj_sum = sums[:, 0:1], sums[:, 1:2]
    total_width = width * lax.axis_size("chan")
    inv_rms = lax.rsqrt(square_sum / total_width + EPSILON)
    normed = (resid * inv_rms * norm_gain).astype(jnp.bfloat16)
    grad_resid = inv_rms * (scaled - resid * inv_rms * inv_rms * (proj_sum / total_width))
    outer_grad = (grad_resid * conv).astype(jnp.bfloat16)
    dconv = grad_resid * outer

    dconv_c = to_channels(dconv.astype(jnp.bfloat16), parts).reshape(rows, tok)
    (grads_c,) = vmem_call(
        backward_kernel,
        (jax.ShapeDtypeStruct((blocks, 2, chans, tok), jnp.bfloat16),),
        [pltpu.VMEM((rows, tok), jnp.float32), pltpu.VMEM((rows, 2 * half), jnp.float32)],
        dconv_c, filt_spec, chan_in, jnp.asarray(forward_np.T), jnp.asarray(inverse_np[:half].T),
    )
    grads = from_channels(grads_c)
    return (normed, grad_resid.astype(jnp.bfloat16), outer_grad, grads[0], grads[1])


def solution(mesh):
    placed = (
        P("seq", "chan"),
        P("seq", "chan"),
        P("seq", "chan"),
        P("seq", "chan"),
        P("seq", "chan"),
        P("chan"),
        P("seq", "chan"),
    )
    return jax.shard_map(
        body,
        mesh=mesh,
        in_specs=placed,
        out_specs=(
            P("seq", "chan"),
            P("seq", "chan"),
            P("seq", "chan"),
            P("seq", "chan"),
            P("seq", "chan"),
        ),
        check_vma=False,
    )
```

```python
import functools
import math

import numpy as np

import jax
import jax.numpy as jnp
from jax import lax
from jax.experimental import pallas as pl
from jax.experimental.pallas import tpu as pltpu
from jax.sharding import PartitionSpec as P

EPSILON = 1e-06
HIGHEST_MODE = lax.Precision.HIGHEST


def dft_tables(half):
    length = 2 * half
    rows = np.arange(length)[:, None]
    cols = np.arange(length)[None, :]
    step = math.pi / half
    phase = (rows % half * cols % length).astype(np.float64) * step
    nyquist = (half * cols % length).astype(np.float64) * step
    forward = np.where(
        rows < half, np.cos(phase), np.where(rows == half, np.cos(nyquist), -np.sin(phase))
    )
    phase_back = (cols % half * rows % length).astype(np.float64) * step
    nyquist_back = (half * rows % length).astype(np.float64) * step
    weight = np.where(cols == 0, 1.0, 2.0)
    inverse = np.where(
        cols < half,
        weight * np.cos(phase_back),
        np.where(cols == half, np.cos(nyquist_back), -2.0 * np.sin(phase_back)),
    )
    return forward.astype(np.float32), (inverse / length).astype(np.float32)


def spectral_product(left, right, conjugate):
    half = left.shape[-1] // 2
    left_real, left_imag = (left[..., :half], left[..., half:])
    right_real, right_imag = (right[..., :half], right[..., half:])
    first_bin = lax.broadcasted_iota(jnp.int32, (1,) * (left.ndim - 1) + (half,), left.ndim - 1) == 0
    if conjugate:
        right_eff = jnp.where(first_bin, right_imag, -right_imag)
    else:
        right_eff = right_imag
    real_out = left_real * right_real - jnp.where(first_bin, 0.0, left_imag * right_eff)
    imag_out = jnp.where(
        first_bin, left_imag * right_imag, left_real * right_eff + left_imag * right_real
    )
    return jnp.concatenate([real_out, imag_out], axis=-1)


def rows_times(left, table):
    return lax.dot_general(
        left, table, (((left.ndim - 1,), (1,)), ((), ())),
        precision=HIGHEST_MODE, preferred_element_type=jnp.float32,
    )


def packed_product(left, right, conjugate):
    half = left.shape[-1] // 2
    left_real, left_imag = (left[:, :half], left[:, half:])
    right_real, right_imag = (right[:, :half], right[:, half:])
    first_bin = lax.broadcasted_iota(jnp.int32, left_real.shape, 1) == 0
    if conjugate:
        right_eff = jnp.where(first_bin, right_imag, -right_imag)
    else:
        right_eff = right_imag
    real_out = left_real * right_real - jnp.where(first_bin, 0.0, left_imag * right_eff)
    imag_out = jnp.where(
        first_bin, left_imag * right_imag, left_real * right_eff + left_imag * right_real
    )
    return real_out, imag_out


def kdot(left, right):
    return jnp.dot(left, right, precision=HIGHEST_MODE, preferred_element_type=jnp.float32)


def tiled_rows(part, count):
    rows, lanes = part.shape
    return jnp.broadcast_to(part[None], (count, rows, lanes)).reshape(count * rows, lanes)


def forward_kernel(x_ref, fwd_ref, inv_ref, conv_ref, filt_ref, acc_ref):
    blocks, _, chans, tok = x_ref.shape
    rows = blocks * chans
    mixed = x_ref[:, 0, :, :].astype(jnp.float32).reshape(rows, tok)
    taps = x_ref[:, 1, :, :].astype(jnp.float32).reshape(rows, tok)
    table = fwd_ref[...]
    data_spec = kdot(mixed, table)
    filt_spec = kdot(taps, table)
    filt_ref[...] = filt_spec
    half = data_spec.shape[1] // 2
    real0, imag0 = packed_product(data_spec, tiled_rows(filt_spec[0:chans], blocks), False)
    acc_ref[:, :half] = real0
    acc_ref[:, half:] = imag0
    for lag in range(1, blocks):
        count = blocks - lag
        real, imag = packed_product(
            data_spec[: count * chans], tiled_rows(filt_spec[lag * chans : (lag + 1) * chans], count), False
        )
        acc_ref[lag * chans :, :half] += real
        acc_ref[lag * chans :, half:] += imag
    waveform = kdot(acc_ref[...], inv_ref[...])
    conv_ref[0:chans, :] = waveform[0:chans, :tok].astype(conv_ref.dtype)
    conv_ref[chans:, :] = (waveform[chans:, :tok] + waveform[: rows - chans, tok:]).astype(conv_ref.dtype)


def backward_kernel(chans, d_ref, filt_ref, fwd_ref, inv_ref, out_ref, fol_ref, acc_ref):
    rows, tok = d_ref.shape
    blocks = rows // chans
    dconv = d_ref[...].astype(jnp.float32)
    fol_ref[: rows - chans, :] = dconv[chans:, :]
    fol_ref[rows - chans :, :] = jnp.zeros((chans, tok), jnp.float32)
    back_spec = kdot(dconv, fwd_ref[:tok, :]) + kdot(fol_ref[...], fwd_ref[tok:, :])
    filt_spec = filt_ref[...]
    half = back_spec.shape[1] // 2
    real0, imag0 = packed_product(back_spec, tiled_rows(filt_spec[0:chans], blocks), True)
    acc_ref[:, :half] = real0
    acc_ref[:, half:] = imag0
    for lag in range(1, blocks):
        count = blocks - lag
        real, imag = packed_product(
            back_spec[lag * chans :], tiled_rows(filt_spec[lag * chans : (lag + 1) * chans], count), True
        )
        acc_ref[: count * chans, :half] += real
        acc_ref[: count * chans, half:] += imag
    out_ref[...] = kdot(acc_ref[...], inv_ref[...]).astype(out_ref.dtype)


def vmem_call(kernel, outs, scratch, *args):
    return pl.pallas_call(
        kernel,
        out_shape=outs,
        in_specs=[pl.BlockSpec(memory_space=pltpu.VMEM) for _ in args],
        out_specs=tuple(pl.BlockSpec(memory_space=pltpu.VMEM) for _ in outs),
        scratch_shapes=scratch,
    )(*args)


def to_channels(x, parts):
    tok, width = x.shape[-2], x.shape[-1]
    lead = x.shape[:-2]
    xt = jnp.swapaxes(x, -1, -2).reshape(lead + (parts, width // parts, tok))
    xt = jnp.moveaxis(xt, len(lead), 0)
    return lax.all_to_all(xt, "seq", 0, 0)


def from_channels(xc):
    back = lax.all_to_all(xc, "seq", 0, 0)
    back = jnp.moveaxis(back, 0, -3)
    shape = back.shape
    back = back.reshape(shape[:-3] + (shape[-3] * shape[-2], shape[-1]))
    return jnp.swapaxes(back, -1, -2)


def chan_sum(partial):
    count = lax.axis_size("chan")
    spread = jnp.broadcast_to(partial[None], (count,) + partial.shape)
    return jnp.sum(lax.all_to_all(spread, "chan", 0, 0), axis=0)


def body(stream_in, outer_gate, inner_gate, values, long_filter, norm_gain, cotangent):
    half = stream_in.shape[0]
    width = stream_in.shape[1]
    parts = lax.axis_size("seq")
    forward_np, inverse_np = dft_tables(half)

    inner = inner_gate.astype(jnp.float32)
    value_rows = values.astype(jnp.float32)
    stacked = jnp.stack([(inner * value_rows).astype(jnp.bfloat16), long_filter], axis=0)
    chan_in = to_channels(stacked, parts)
    blocks, _, chans, tok = chan_in.shape
    rows = blocks * chans
    conv_c, filt_spec = vmem_call(
        forward_kernel,
        (
            jax.ShapeDtypeStruct((rows, tok), jnp.bfloat16),
            jax.ShapeDtypeStruct((rows, 2 * half), jnp.float32),
        ),
        [pltpu.VMEM((rows, 2 * half), jnp.float32)],
        chan_in, jnp.asarray(forward_np[:, :half].T), jnp.asarray(inverse_np.T),
    )
    conv_c = conv_c.reshape(blocks, chans, tok)
    conv = from_channels(conv_c).astype(jnp.float32)

    outer = outer_gate.astype(jnp.float32)
    resid = stream_in.astype(jnp.float32) + outer * conv
    scaled = cotangent.astype(jnp.float32) * norm_gain
    sums = chan_sum(
        jnp.concatenate(
            [
                jnp.sum(resid * resid, axis=1, keepdims=True),
                jnp.sum(scaled * resid, axis=1, keepdims=True),
            ],
            axis=1,
        )
    )
    square_sum, proj_sum = sums[:, 0:1], sums[:, 1:2]
    total_width = width * lax.axis_size("chan")
    inv_rms = lax.rsqrt(square_sum / total_width + EPSILON)
    normed = (resid * inv_rms * norm_gain).astype(jnp.bfloat16)
    grad_resid = inv_rms * (scaled - resid * inv_rms * inv_rms * (proj_sum / total_width))
    outer_grad = (grad_resid * conv).astype(jnp.bfloat16)
    dconv = grad_resid * outer

    dconv_c = to_channels(dconv.astype(jnp.bfloat16), parts).reshape(rows, tok)
    (dmixed_c,) = vmem_call(
        functools.partial(backward_kernel, chans),
        (jax.ShapeDtypeStruct((rows, tok), jnp.bfloat16),),
        [pltpu.VMEM((rows, tok), jnp.float32), pltpu.VMEM((rows, 2 * half), jnp.float32)],
        dconv_c, filt_spec, jnp.asarray(forward_np.T), jnp.asarray(inverse_np[:half].T),
    )
    dmixed = from_channels(dmixed_c.reshape(blocks, chans, tok)).astype(jnp.float32)
    inner_grad = (dmixed * value_rows).astype(jnp.bfloat16)
    value_grad = (dmixed * inner).astype(jnp.bfloat16)
    return (normed, grad_resid.astype(jnp.bfloat16), outer_grad, inner_grad, value_grad)


def solution(mesh):
    placed = (
        P("seq", "chan"),
        P("seq", "chan"),
        P("seq", "chan"),
        P("seq", "chan"),
        P("seq", "chan"),
        P("chan"),
        P("seq", "chan"),
    )
    return jax.shard_map(
        body,
        mesh=mesh,
        in_specs=placed,
        out_specs=(
            P("seq", "chan"),
            P("seq", "chan"),
            P("seq", "chan"),
            P("seq", "chan"),
            P("seq", "chan"),
        ),
        check_vma=False,
    )
```

```python
import functools
import math

import numpy as np

import jax
import jax.numpy as jnp
from jax import lax
from jax.experimental import pallas as pl
from jax.experimental.pallas import tpu as pltpu
from jax.sharding import PartitionSpec as P

EPSILON = 1e-06
HIGHEST_MODE = lax.Precision.HIGHEST


def dft_tables(half):
    length = 2 * half
    rows = np.arange(length)[:, None]
    cols = np.arange(length)[None, :]
    step = math.pi / half
    phase = (rows % half * cols % length).astype(np.float64) * step
    nyquist = (half * cols % length).astype(np.float64) * step
    forward = np.where(
        rows < half, np.cos(phase), np.where(rows == half, np.cos(nyquist), -np.sin(phase))
    )
    phase_back = (cols % half * rows % length).astype(np.float64) * step
    nyquist_back = (half * rows % length).astype(np.float64) * step
    weight = np.where(cols == 0, 1.0, 2.0)
    inverse = np.where(
        cols < half,
        weight * np.cos(phase_back),
        np.where(cols == half, np.cos(nyquist_back), -2.0 * np.sin(phase_back)),
    )
    return forward.astype(np.float32), (inverse / length).astype(np.float32)


def spectral_product(left, right, conjugate):
    half = left.shape[-1] // 2
    left_real, left_imag = (left[..., :half], left[..., half:])
    right_real, right_imag = (right[..., :half], right[..., half:])
    first_bin = lax.broadcasted_iota(jnp.int32, (1,) * (left.ndim - 1) + (half,), left.ndim - 1) == 0
    if conjugate:
        right_eff = jnp.where(first_bin, right_imag, -right_imag)
    else:
        right_eff = right_imag
    real_out = left_real * right_real - jnp.where(first_bin, 0.0, left_imag * right_eff)
    imag_out = jnp.where(
        first_bin, left_imag * right_imag, left_real * right_eff + left_imag * right_real
    )
    return jnp.concatenate([real_out, imag_out], axis=-1)


def rows_times(left, table):
    return lax.dot_general(
        left, table, (((left.ndim - 1,), (1,)), ((), ())),
        precision=HIGHEST_MODE, preferred_element_type=jnp.float32,
    )


def packed_product(left, right, conjugate):
    half = left.shape[-1] // 2
    left_real, left_imag = (left[:, :half], left[:, half:])
    right_real, right_imag = (right[:, :half], right[:, half:])
    first_bin = lax.broadcasted_iota(jnp.int32, left_real.shape, 1) == 0
    if conjugate:
        right_eff = jnp.where(first_bin, right_imag, -right_imag)
    else:
        right_eff = right_imag
    real_out = left_real * right_real - jnp.where(first_bin, 0.0, left_imag * right_eff)
    imag_out = jnp.where(
        first_bin, left_imag * right_imag, left_real * right_eff + left_imag * right_real
    )
    return real_out, imag_out


def kdot(left, right):
    return jnp.dot(left, right, precision=HIGHEST_MODE, preferred_element_type=jnp.float32)


def tiled_rows(part, count):
    rows, lanes = part.shape
    return jnp.broadcast_to(part[None], (count, rows, lanes)).reshape(count * rows, lanes)


def forward_kernel(x_ref, fwd_ref, inv_ref, conv_ref, filt_ref, acc_ref):
    blocks, _, chans, tok = x_ref.shape
    rows = blocks * chans
    mixed = x_ref[:, 0, :, :].astype(jnp.float32).reshape(rows, tok)
    taps = x_ref[:, 1, :, :].astype(jnp.float32).reshape(rows, tok)
    table = fwd_ref[...]
    data_spec = kdot(mixed, table)
    filt_spec = kdot(taps, table)
    filt_ref[...] = filt_spec
    half = data_spec.shape[1] // 2
    real0, imag0 = packed_product(data_spec, tiled_rows(filt_spec[0:chans], blocks), False)
    acc_ref[:, :half] = real0
    acc_ref[:, half:] = imag0
    for lag in range(1, blocks):
        count = blocks - lag
        real, imag = packed_product(
            data_spec[: count * chans], tiled_rows(filt_spec[lag * chans : (lag + 1) * chans], count), False
        )
        acc_ref[lag * chans :, :half] += real
        acc_ref[lag * chans :, half:] += imag
    waveform = kdot(acc_ref[...], inv_ref[...])
    conv_ref[0:chans, :] = waveform[0:chans, :tok].astype(conv_ref.dtype)
    conv_ref[chans:, :] = (waveform[chans:, :tok] + waveform[: rows - chans, tok:]).astype(conv_ref.dtype)


def backward_kernel(chans, d_ref, filt_ref, fwd_ref, inv_ref, out_ref, fol_ref, acc_ref):
    rows, tok = d_ref.shape
    blocks = rows // chans
    dconv = d_ref[...].astype(jnp.float32)
    fol_ref[: rows - chans, :] = dconv[chans:, :]
    fol_ref[rows - chans :, :] = jnp.zeros((chans, tok), jnp.float32)
    back_spec = kdot(dconv, fwd_ref[:tok, :]) + kdot(fol_ref[...], fwd_ref[tok:, :])
    filt_spec = filt_ref[...]
    half = back_spec.shape[1] // 2
    real0, imag0 = packed_product(back_spec, tiled_rows(filt_spec[0:chans], blocks), True)
    acc_ref[:, :half] = real0
    acc_ref[:, half:] = imag0
    for lag in range(1, blocks):
        count = blocks - lag
        real, imag = packed_product(
            back_spec[lag * chans :], tiled_rows(filt_spec[lag * chans : (lag + 1) * chans], count), True
        )
        acc_ref[: count * chans, :half] += real
        acc_ref[: count * chans, half:] += imag
    out_ref[...] = kdot(acc_ref[...], inv_ref[...]).astype(out_ref.dtype)


def head_kernel(inner_ref, values_ref, filt_ref, out_ref):
    blocks, _, chans, tok = out_ref.shape
    mixed = (inner_ref[...].astype(jnp.float32) * values_ref[...].astype(jnp.float32)).astype(jnp.bfloat16)
    out_ref[:, 0, :, :] = mixed.astype(jnp.float32).T.reshape(blocks, chans, tok).astype(jnp.bfloat16)
    out_ref[:, 1, :, :] = filt_ref[...].astype(jnp.float32).T.reshape(blocks, chans, tok).astype(jnp.bfloat16)


def tail_kernel(d_ref, inner_ref, values_ref, inner_grad_ref, value_grad_ref):
    blocks, chans, tok = d_ref.shape
    dmixed = d_ref[...].astype(jnp.float32).reshape(blocks * chans, tok).T
    inner_grad_ref[...] = (dmixed * values_ref[...].astype(jnp.float32)).astype(inner_grad_ref.dtype)
    value_grad_ref[...] = (dmixed * inner_ref[...].astype(jnp.float32)).astype(value_grad_ref.dtype)


def vmem_call(kernel, outs, scratch, *args):
    return pl.pallas_call(
        kernel,
        out_shape=outs,
        in_specs=[pl.BlockSpec(memory_space=pltpu.VMEM) for _ in args],
        out_specs=tuple(pl.BlockSpec(memory_space=pltpu.VMEM) for _ in outs),
        scratch_shapes=scratch,
    )(*args)


def to_channels(x, parts):
    tok, width = x.shape[-2], x.shape[-1]
    lead = x.shape[:-2]
    xt = jnp.swapaxes(x, -1, -2).reshape(lead + (parts, width // parts, tok))
    xt = jnp.moveaxis(xt, len(lead), 0)
    return lax.all_to_all(xt, "seq", 0, 0)


def from_channels(xc):
    back = lax.all_to_all(xc, "seq", 0, 0)
    back = jnp.moveaxis(back, 0, -3)
    shape = back.shape
    back = back.reshape(shape[:-3] + (shape[-3] * shape[-2], shape[-1]))
    return jnp.swapaxes(back, -1, -2)


def chan_sum(partial):
    count = lax.axis_size("chan")
    spread = jnp.broadcast_to(partial[None], (count,) + partial.shape)
    return jnp.sum(lax.all_to_all(spread, "chan", 0, 0), axis=0)


def body(stream_in, outer_gate, inner_gate, values, long_filter, norm_gain, cotangent):
    half = stream_in.shape[0]
    width = stream_in.shape[1]
    parts = lax.axis_size("seq")
    forward_np, inverse_np = dft_tables(half)

    (stacked,) = vmem_call(
        head_kernel,
        (jax.ShapeDtypeStruct((parts, 2, width // parts, half), jnp.bfloat16),),
        [],
        inner_gate, values, long_filter,
    )
    chan_in = lax.all_to_all(stacked, "seq", 0, 0)
    blocks, _, chans, tok = chan_in.shape
    rows = blocks * chans
    conv_c, filt_spec = vmem_call(
        forward_kernel,
        (
            jax.ShapeDtypeStruct((rows, tok), jnp.bfloat16),
            jax.ShapeDtypeStruct((rows, 2 * half), jnp.float32),
        ),
        [pltpu.VMEM((rows, 2 * half), jnp.float32)],
        chan_in, jnp.asarray(forward_np[:, :half].T), jnp.asarray(inverse_np.T),
    )
    conv_c = conv_c.reshape(blocks, chans, tok)
    conv = from_channels(conv_c).astype(jnp.float32)

    outer = outer_gate.astype(jnp.float32)
    resid = stream_in.astype(jnp.float32) + outer * conv
    scaled = cotangent.astype(jnp.float32) * norm_gain
    sums = chan_sum(
        jnp.concatenate(
            [
                jnp.sum(resid * resid, axis=1, keepdims=True),
                jnp.sum(scaled * resid, axis=1, keepdims=True),
            ],
            axis=1,
        )
    )
    square_sum, proj_sum = sums[:, 0:1], sums[:, 1:2]
    total_width = width * lax.axis_size("chan")
    inv_rms = lax.rsqrt(square_sum / total_width + EPSILON)
    normed = (resid * inv_rms * norm_gain).astype(jnp.bfloat16)
    grad_resid = inv_rms * (scaled - resid * inv_rms * inv_rms * (proj_sum / total_width))
    outer_grad = (grad_resid * conv).astype(jnp.bfloat16)
    dconv = grad_resid * outer

    dconv_c = to_channels(dconv.astype(jnp.bfloat16), parts).reshape(rows, tok)
    (dmixed_c,) = vmem_call(
        functools.partial(backward_kernel, chans),
        (jax.ShapeDtypeStruct((rows, tok), jnp.bfloat16),),
        [pltpu.VMEM((rows, tok), jnp.float32), pltpu.VMEM((rows, 2 * half), jnp.float32)],
        dconv_c, filt_spec, jnp.asarray(forward_np.T), jnp.asarray(inverse_np[:half].T),
    )
    dmixed_t = lax.all_to_all(dmixed_c.reshape(blocks, chans, tok), "seq", 0, 0)
    inner_grad, value_grad = vmem_call(
        tail_kernel,
        (
            jax.ShapeDtypeStruct((half, width), jnp.bfloat16),
            jax.ShapeDtypeStruct((half, width), jnp.bfloat16),
        ),
        [],
        dmixed_t, inner_gate, values,
    )
    return (normed, grad_resid.astype(jnp.bfloat16), outer_grad, inner_grad, value_grad)


def solution(mesh):
    placed = (
        P("seq", "chan"),
        P("seq", "chan"),
        P("seq", "chan"),
        P("seq", "chan"),
        P("seq", "chan"),
        P("chan"),
        P("seq", "chan"),
    )
    return jax.shard_map(
        body,
        mesh=mesh,
        in_specs=placed,
        out_specs=(
            P("seq", "chan"),
            P("seq", "chan"),
            P("seq", "chan"),
            P("seq", "chan"),
            P("seq", "chan"),
        ),
        check_vma=False,
    )
```

```python
import functools
import math

import numpy as np

import jax
import jax.numpy as jnp
from jax import lax
from jax.experimental import pallas as pl
from jax.experimental.pallas import tpu as pltpu
from jax.sharding import PartitionSpec as P

EPSILON = 1e-06
HIGHEST_MODE = lax.Precision.HIGHEST


def dft_tables(half):
    length = 2 * half
    rows = np.arange(length)[:, None]
    cols = np.arange(length)[None, :]
    step = math.pi / half
    phase = (rows % half * cols % length).astype(np.float64) * step
    nyquist = (half * cols % length).astype(np.float64) * step
    forward = np.where(
        rows < half, np.cos(phase), np.where(rows == half, np.cos(nyquist), -np.sin(phase))
    )
    phase_back = (cols % half * rows % length).astype(np.float64) * step
    nyquist_back = (half * rows % length).astype(np.float64) * step
    weight = np.where(cols == 0, 1.0, 2.0)
    inverse = np.where(
        cols < half,
        weight * np.cos(phase_back),
        np.where(cols == half, np.cos(nyquist_back), -2.0 * np.sin(phase_back)),
    )
    return forward.astype(np.float32), (inverse / length).astype(np.float32)


def spectral_product(left, right, conjugate):
    half = left.shape[-1] // 2
    left_real, left_imag = (left[..., :half], left[..., half:])
    right_real, right_imag = (right[..., :half], right[..., half:])
    first_bin = lax.broadcasted_iota(jnp.int32, (1,) * (left.ndim - 1) + (half,), left.ndim - 1) == 0
    if conjugate:
        right_eff = jnp.where(first_bin, right_imag, -right_imag)
    else:
        right_eff = right_imag
    real_out = left_real * right_real - jnp.where(first_bin, 0.0, left_imag * right_eff)
    imag_out = jnp.where(
        first_bin, left_imag * right_imag, left_real * right_eff + left_imag * right_real
    )
    return jnp.concatenate([real_out, imag_out], axis=-1)


def rows_times(left, table):
    return lax.dot_general(
        left, table, (((left.ndim - 1,), (1,)), ((), ())),
        precision=HIGHEST_MODE, preferred_element_type=jnp.float32,
    )


def kdot(left, right):
    return jnp.dot(left, right, precision=lax.Precision.HIGH, preferred_element_type=jnp.float32)


def split_taps(filt_spec, fr_ref, ff_ref, fm_ref):
    half = filt_spec.shape[1] // 2
    real, imag = filt_spec[:, :half], filt_spec[:, half:]
    first_bin = lax.broadcasted_iota(jnp.int32, real.shape, 1) == 0
    fr_ref[...] = real
    ff_ref[...] = jnp.where(first_bin, imag, real)
    fm_ref[...] = jnp.where(first_bin, 0.0, imag)


def block_terms(spec_ref, fr_ref, ff_ref, fm_ref, acc_ref, chans, pairs, conjugate):
    half = acc_ref.shape[1] // 2
    for out, terms in pairs:
        acc_real = jnp.zeros((chans, half), jnp.float32)
        acc_imag = jnp.zeros((chans, half), jnp.float32)
        for src, lag in terms:
            rows = pl.ds(src * chans, chans)
            taps = pl.ds(lag * chans, chans)
            left_real = spec_ref[rows, pl.ds(0, half)]
            left_imag = spec_ref[rows, pl.ds(half, half)]
            right_real = fr_ref[taps, :]
            right_first = ff_ref[taps, :]
            right_masked = fm_ref[taps, :]
            if conjugate:
                acc_real = acc_real + (left_real * right_real + left_imag * right_masked)
                acc_imag = acc_imag + (left_imag * right_first - left_real * right_masked)
            else:
                acc_real = acc_real + (left_real * right_real - left_imag * right_masked)
                acc_imag = acc_imag + (left_real * right_masked + left_imag * right_first)
        acc_ref[pl.ds(out * chans, chans), pl.ds(0, half)] = acc_real
        acc_ref[pl.ds(out * chans, chans), pl.ds(half, half)] = acc_imag


def forward_kernel(x_ref, fwd_ref, inv_ref, conv_ref, filt_ref, spec_ref, fr_ref, ff_ref, fm_ref, acc_ref):
    blocks, _, chans, tok = x_ref.shape
    rows = blocks * chans
    mixed = x_ref[:, 0, :, :].astype(jnp.float32).reshape(rows, tok)
    taps = x_ref[:, 1, :, :].astype(jnp.float32).reshape(rows, tok)
    table = fwd_ref[...]
    spec_ref[...] = kdot(mixed, table)
    filt_spec = kdot(taps, table)
    filt_ref[...] = filt_spec
    split_taps(filt_spec, fr_ref, ff_ref, fm_ref)
    pairs = [(out, [(out - lag, lag) for lag in range(out + 1)]) for out in range(blocks)]
    block_terms(spec_ref, fr_ref, ff_ref, fm_ref, acc_ref, chans, pairs, False)
    waveform = kdot(acc_ref[...], inv_ref[...])
    conv_ref[0:chans, :] = waveform[0:chans, :tok].astype(conv_ref.dtype)
    conv_ref[chans:, :] = (waveform[chans:, :tok] + waveform[: rows - chans, tok:]).astype(conv_ref.dtype)


def backward_kernel(chans, d_ref, filt_ref, fwd_ref, inv_ref, out_ref, fol_ref, spec_ref, fr_ref, ff_ref, fm_ref, acc_ref):
    rows, tok = d_ref.shape
    blocks = rows // chans
    dconv = d_ref[...].astype(jnp.float32)
    fol_ref[: rows - chans, :] = dconv[chans:, :]
    fol_ref[rows - chans :, :] = jnp.zeros((chans, tok), jnp.float32)
    spec_ref[...] = kdot(dconv, fwd_ref[:tok, :]) + kdot(fol_ref[...], fwd_ref[tok:, :])
    split_taps(filt_ref[...], fr_ref, ff_ref, fm_ref)
    pairs = [(out, [(out + lag, lag) for lag in range(blocks - out)]) for out in range(blocks)]
    block_terms(spec_ref, fr_ref, ff_ref, fm_ref, acc_ref, chans, pairs, True)
    out_ref[...] = kdot(acc_ref[...], inv_ref[...]).astype(out_ref.dtype)


def vmem_call(kernel, outs, scratch, *args):
    return pl.pallas_call(
        kernel,
        out_shape=outs,
        in_specs=[pl.BlockSpec(memory_space=pltpu.VMEM) for _ in args],
        out_specs=tuple(pl.BlockSpec(memory_space=pltpu.VMEM) for _ in outs),
        scratch_shapes=scratch,
    )(*args)


def to_channels(x, parts):
    tok, width = x.shape[-2], x.shape[-1]
    lead = x.shape[:-2]
    xt = jnp.swapaxes(x, -1, -2).reshape(lead + (parts, width // parts, tok))
    xt = jnp.moveaxis(xt, len(lead), 0)
    return lax.all_to_all(xt, "seq", 0, 0)


def from_channels(xc):
    back = lax.all_to_all(xc, "seq", 0, 0)
    back = jnp.moveaxis(back, 0, -3)
    shape = back.shape
    back = back.reshape(shape[:-3] + (shape[-3] * shape[-2], shape[-1]))
    return jnp.swapaxes(back, -1, -2)


def chan_sum(partial):
    count = lax.axis_size("chan")
    spread = jnp.broadcast_to(partial[None], (count,) + partial.shape)
    return jnp.sum(lax.all_to_all(spread, "chan", 0, 0), axis=0)


def body(stream_in, outer_gate, inner_gate, values, long_filter, norm_gain, cotangent):
    half = stream_in.shape[0]
    width = stream_in.shape[1]
    parts = lax.axis_size("seq")
    forward_np, inverse_np = dft_tables(half)

    inner = inner_gate.astype(jnp.float32)
    value_rows = values.astype(jnp.float32)
    stacked = jnp.stack([(inner * value_rows).astype(jnp.bfloat16), long_filter], axis=0)
    chan_in = to_channels(stacked, parts)
    blocks, _, chans, tok = chan_in.shape
    rows = blocks * chans
    conv_c, filt_spec = vmem_call(
        forward_kernel,
        (
            jax.ShapeDtypeStruct((rows, tok), jnp.bfloat16),
            jax.ShapeDtypeStruct((rows, 2 * half), jnp.float32),
        ),
        [pltpu.VMEM((rows, 2 * half), jnp.float32)]
        + [pltpu.VMEM((rows, half), jnp.float32) for _ in range(3)]
        + [pltpu.VMEM((rows, 2 * half), jnp.float32)],
        chan_in, jnp.asarray(forward_np[:, :half].T), jnp.asarray(inverse_np.T),
    )
    conv_c = conv_c.reshape(blocks, chans, tok)
    conv = from_channels(conv_c).astype(jnp.float32)

    outer = outer_gate.astype(jnp.float32)
    resid = stream_in.astype(jnp.float32) + outer * conv
    scaled = cotangent.astype(jnp.float32) * norm_gain
    sums = chan_sum(
        jnp.concatenate(
            [
                jnp.sum(resid * resid, axis=1, keepdims=True),
                jnp.sum(scaled * resid, axis=1, keepdims=True),
            ],
            axis=1,
        )
    )
    square_sum, proj_sum = sums[:, 0:1], sums[:, 1:2]
    total_width = width * lax.axis_size("chan")
    inv_rms = lax.rsqrt(square_sum / total_width + EPSILON)
    normed = (resid * inv_rms * norm_gain).astype(jnp.bfloat16)
    grad_resid = inv_rms * (scaled - resid * inv_rms * inv_rms * (proj_sum / total_width))
    outer_grad = (grad_resid * conv).astype(jnp.bfloat16)
    dconv = grad_resid * outer

    dconv_c = to_channels(dconv.astype(jnp.bfloat16), parts).reshape(rows, tok)
    (dmixed_c,) = vmem_call(
        functools.partial(backward_kernel, chans),
        (jax.ShapeDtypeStruct((rows, tok), jnp.bfloat16),),
        [pltpu.VMEM((rows, tok), jnp.float32), pltpu.VMEM((rows, 2 * half), jnp.float32)]
        + [pltpu.VMEM((rows, half), jnp.float32) for _ in range(3)]
        + [pltpu.VMEM((rows, 2 * half), jnp.float32)],
        dconv_c, filt_spec, jnp.asarray(forward_np.T), jnp.asarray(inverse_np[:half].T),
    )
    dmixed = from_channels(dmixed_c.reshape(blocks, chans, tok)).astype(jnp.float32)
    inner_grad = (dmixed * value_rows).astype(jnp.bfloat16)
    value_grad = (dmixed * inner).astype(jnp.bfloat16)
    return (normed, grad_resid.astype(jnp.bfloat16), outer_grad, inner_grad, value_grad)


def solution(mesh):
    placed = (
        P("seq", "chan"),
        P("seq", "chan"),
        P("seq", "chan"),
        P("seq", "chan"),
        P("seq", "chan"),
        P("chan"),
        P("seq", "chan"),
    )
    return jax.shard_map(
        body,
        mesh=mesh,
        in_specs=placed,
        out_specs=(
            P("seq", "chan"),
            P("seq", "chan"),
            P("seq", "chan"),
            P("seq", "chan"),
            P("seq", "chan"),
        ),
        check_vma=False,
    )
```

```python
import functools
import math

import numpy as np

import jax
import jax.numpy as jnp
from jax import lax
from jax.experimental import pallas as pl
from jax.experimental.pallas import tpu as pltpu
from jax.sharding import PartitionSpec as P

EPSILON = 1e-06
HIGHEST_MODE = lax.Precision.HIGHEST


def dft_tables(half):
    length = 2 * half
    rows = np.arange(length)[:, None]
    cols = np.arange(length)[None, :]
    step = math.pi / half
    phase = (rows % half * cols % length).astype(np.float64) * step
    nyquist = (half * cols % length).astype(np.float64) * step
    forward = np.where(
        rows < half, np.cos(phase), np.where(rows == half, np.cos(nyquist), -np.sin(phase))
    )
    phase_back = (cols % half * rows % length).astype(np.float64) * step
    nyquist_back = (half * rows % length).astype(np.float64) * step
    weight = np.where(cols == 0, 1.0, 2.0)
    inverse = np.where(
        cols < half,
        weight * np.cos(phase_back),
        np.where(cols == half, np.cos(nyquist_back), -2.0 * np.sin(phase_back)),
    )
    return forward.astype(np.float32), (inverse / length).astype(np.float32)


def spectral_product(left, right, conjugate):
    half = left.shape[-1] // 2
    left_real, left_imag = (left[..., :half], left[..., half:])
    right_real, right_imag = (right[..., :half], right[..., half:])
    first_bin = lax.broadcasted_iota(jnp.int32, (1,) * (left.ndim - 1) + (half,), left.ndim - 1) == 0
    if conjugate:
        right_eff = jnp.where(first_bin, right_imag, -right_imag)
    else:
        right_eff = right_imag
    real_out = left_real * right_real - jnp.where(first_bin, 0.0, left_imag * right_eff)
    imag_out = jnp.where(
        first_bin, left_imag * right_imag, left_real * right_eff + left_imag * right_real
    )
    return jnp.concatenate([real_out, imag_out], axis=-1)


def rows_times(left, table):
    return lax.dot_general(
        left, table, (((left.ndim - 1,), (1,)), ((), ())),
        precision=HIGHEST_MODE, preferred_element_type=jnp.float32,
    )


def kdot(left, right):
    return jnp.dot(left, right, precision=lax.Precision.HIGH, preferred_element_type=jnp.float32)


def split_taps(filt_spec, fr_ref, ff_ref, fm_ref):
    half = filt_spec.shape[1] // 2
    real, imag = filt_spec[:, :half], filt_spec[:, half:]
    first_bin = lax.broadcasted_iota(jnp.int32, real.shape, 1) == 0
    fr_ref[...] = real
    ff_ref[...] = jnp.where(first_bin, imag, real)
    fm_ref[...] = jnp.where(first_bin, 0.0, imag)


def block_terms(spec_ref, fr_ref, ff_ref, fm_ref, acc_ref, chans, pairs, conjugate):
    half = acc_ref.shape[1] // 2
    for out, terms in pairs:
        acc_real = jnp.zeros((chans, half), jnp.float32)
        acc_imag = jnp.zeros((chans, half), jnp.float32)
        for src, lag in terms:
            rows = pl.ds(src * chans, chans)
            taps = pl.ds(lag * chans, chans)
            left_real = spec_ref[rows, pl.ds(0, half)]
            left_imag = spec_ref[rows, pl.ds(half, half)]
            right_real = fr_ref[taps, :]
            right_first = ff_ref[taps, :]
            right_masked = fm_ref[taps, :]
            if conjugate:
                acc_real = acc_real + (left_real * right_real + left_imag * right_masked)
                acc_imag = acc_imag + (left_imag * right_first - left_real * right_masked)
            else:
                acc_real = acc_real + (left_real * right_real - left_imag * right_masked)
                acc_imag = acc_imag + (left_real * right_masked + left_imag * right_first)
        acc_ref[pl.ds(out * chans, chans), pl.ds(0, half)] = acc_real
        acc_ref[pl.ds(out * chans, chans), pl.ds(half, half)] = acc_imag


def forward_kernel(x_ref, fwd_ref, inv_ref, conv_ref, filt_ref, spec_ref, fr_ref, ff_ref, fm_ref, acc_ref):
    blocks, _, chans, tok = x_ref.shape
    rows = blocks * chans
    mixed = x_ref[:, 0, :, :].astype(jnp.float32).reshape(rows, tok)
    taps = x_ref[:, 1, :, :].astype(jnp.float32).reshape(rows, tok)
    table = fwd_ref[...]
    spec_ref[...] = kdot(mixed, table)
    filt_spec = kdot(taps, table)
    filt_ref[...] = filt_spec
    split_taps(filt_spec, fr_ref, ff_ref, fm_ref)
    pairs = [(out, [(out - lag, lag) for lag in range(out + 1)]) for out in range(blocks)]
    block_terms(spec_ref, fr_ref, ff_ref, fm_ref, acc_ref, chans, pairs, False)
    waveform = kdot(acc_ref[...], inv_ref[...])
    conv_ref[0:chans, :] = waveform[0:chans, :tok].astype(conv_ref.dtype)
    conv_ref[chans:, :] = (waveform[chans:, :tok] + waveform[: rows - chans, tok:]).astype(conv_ref.dtype)


def backward_kernel(chans, d_ref, filt_ref, fwd_ref, inv_ref, out_ref, fol_ref, spec_ref, fr_ref, ff_ref, fm_ref, acc_ref):
    rows, tok = d_ref.shape
    blocks = rows // chans
    dconv = d_ref[...].astype(jnp.float32)
    fol_ref[: rows - chans, :] = dconv[chans:, :]
    fol_ref[rows - chans :, :] = jnp.zeros((chans, tok), jnp.float32)
    spec_ref[...] = kdot(dconv, fwd_ref[:tok, :]) + kdot(fol_ref[...], fwd_ref[tok:, :])
    split_taps(filt_ref[...], fr_ref, ff_ref, fm_ref)
    pairs = [(out, [(out + lag, lag) for lag in range(blocks - out)]) for out in range(blocks)]
    block_terms(spec_ref, fr_ref, ff_ref, fm_ref, acc_ref, chans, pairs, True)
    out_ref[...] = kdot(acc_ref[...], inv_ref[...]).astype(out_ref.dtype)


def vmem_call(kernel, outs, scratch, *args):
    return pl.pallas_call(
        kernel,
        out_shape=outs,
        in_specs=[pl.BlockSpec(memory_space=pltpu.VMEM) for _ in args],
        out_specs=tuple(pl.BlockSpec(memory_space=pltpu.VMEM) for _ in outs),
        scratch_shapes=scratch,
    )(*args)


def to_channels(x, parts):
    tok, width = x.shape[-2], x.shape[-1]
    lead = x.shape[:-2]
    xt = jnp.swapaxes(x, -1, -2).reshape(lead + (parts, width // parts, tok))
    xt = jnp.moveaxis(xt, len(lead), 0)
    return lax.all_to_all(xt, "seq", 0, 0)


def from_channels(xc):
    back = lax.all_to_all(xc, "seq", 0, 0)
    back = jnp.moveaxis(back, 0, -3)
    shape = back.shape
    back = back.reshape(shape[:-3] + (shape[-3] * shape[-2], shape[-1]))
    return jnp.swapaxes(back, -1, -2)


def chan_sum(partial):
    count = lax.axis_size("chan")
    spread = jnp.broadcast_to(partial[None], (count,) + partial.shape)
    return jnp.sum(lax.all_to_all(spread, "chan", 0, 0), axis=0)


def body(stream_in, outer_gate, inner_gate, values, long_filter, norm_gain, cotangent):
    half = stream_in.shape[0]
    width = stream_in.shape[1]
    parts = lax.axis_size("seq")
    forward_np, inverse_np = dft_tables(half)

    inner = inner_gate.astype(jnp.float32)
    value_rows = values.astype(jnp.float32)
    eye = jnp.eye(width, dtype=jnp.bfloat16)

    def flipped(x):
        return lax.dot_general(eye, x, (((1,), (1,)), ((), ())), preferred_element_type=jnp.float32)

    stacked = jnp.stack(
        [flipped((inner * value_rows).astype(jnp.bfloat16)), flipped(long_filter)], axis=0
    ).astype(jnp.bfloat16)
    stacked = jnp.moveaxis(stacked.reshape(2, parts, width // parts, half), 1, 0)
    chan_in = lax.all_to_all(stacked, "seq", 0, 0)
    blocks, _, chans, tok = chan_in.shape
    rows = blocks * chans
    conv_c, filt_spec = vmem_call(
        forward_kernel,
        (
            jax.ShapeDtypeStruct((rows, tok), jnp.bfloat16),
            jax.ShapeDtypeStruct((rows, 2 * half), jnp.float32),
        ),
        [pltpu.VMEM((rows, 2 * half), jnp.float32)]
        + [pltpu.VMEM((rows, half), jnp.float32) for _ in range(3)]
        + [pltpu.VMEM((rows, 2 * half), jnp.float32)],
        chan_in, jnp.asarray(forward_np[:, :half].T), jnp.asarray(inverse_np.T),
    )
    conv_c = conv_c.reshape(blocks, chans, tok)
    conv = from_channels(conv_c).astype(jnp.float32)

    outer = outer_gate.astype(jnp.float32)
    resid = stream_in.astype(jnp.float32) + outer * conv
    scaled = cotangent.astype(jnp.float32) * norm_gain
    sums = chan_sum(
        jnp.concatenate(
            [
                jnp.sum(resid * resid, axis=1, keepdims=True),
                jnp.sum(scaled * resid, axis=1, keepdims=True),
            ],
            axis=1,
        )
    )
    square_sum, proj_sum = sums[:, 0:1], sums[:, 1:2]
    total_width = width * lax.axis_size("chan")
    inv_rms = lax.rsqrt(square_sum / total_width + EPSILON)
    normed = (resid * inv_rms * norm_gain).astype(jnp.bfloat16)
    grad_resid = inv_rms * (scaled - resid * inv_rms * inv_rms * (proj_sum / total_width))
    outer_grad = (grad_resid * conv).astype(jnp.bfloat16)
    dconv = grad_resid * outer

    dconv_c = to_channels(dconv.astype(jnp.bfloat16), parts).reshape(rows, tok)
    (dmixed_c,) = vmem_call(
        functools.partial(backward_kernel, chans),
        (jax.ShapeDtypeStruct((rows, tok), jnp.bfloat16),),
        [pltpu.VMEM((rows, tok), jnp.float32), pltpu.VMEM((rows, 2 * half), jnp.float32)]
        + [pltpu.VMEM((rows, half), jnp.float32) for _ in range(3)]
        + [pltpu.VMEM((rows, 2 * half), jnp.float32)],
        dconv_c, filt_spec, jnp.asarray(forward_np.T), jnp.asarray(inverse_np[:half].T),
    )
    dmixed_t = lax.all_to_all(dmixed_c.reshape(blocks, chans, tok), "seq", 0, 0).reshape(width, tok)
    dmixed = lax.dot_general(dmixed_t, eye, (((0,), (0,)), ((), ())), preferred_element_type=jnp.float32)
    inner_grad = (dmixed * value_rows).astype(jnp.bfloat16)
    value_grad = (dmixed * inner).astype(jnp.bfloat16)
    return (normed, grad_resid.astype(jnp.bfloat16), outer_grad, inner_grad, value_grad)


def solution(mesh):
    placed = (
        P("seq", "chan"),
        P("seq", "chan"),
        P("seq", "chan"),
        P("seq", "chan"),
        P("seq", "chan"),
        P("chan"),
        P("seq", "chan"),
    )
    return jax.shard_map(
        body,
        mesh=mesh,
        in_specs=placed,
        out_specs=(
            P("seq", "chan"),
            P("seq", "chan"),
            P("seq", "chan"),
            P("seq", "chan"),
            P("seq", "chan"),
        ),
        check_vma=False,
    )
```

```python
import functools
import math

import numpy as np

import jax
import jax.numpy as jnp
from jax import lax
from jax.experimental import pallas as pl
from jax.experimental.pallas import tpu as pltpu
from jax.sharding import PartitionSpec as P

EPSILON = 1e-06
HIGHEST_MODE = lax.Precision.HIGHEST


def dft_tables(half):
    length = 2 * half
    rows = np.arange(length)[:, None]
    cols = np.arange(length)[None, :]
    step = math.pi / half
    phase = (rows % half * cols % length).astype(np.float64) * step
    nyquist = (half * cols % length).astype(np.float64) * step
    forward = np.where(
        rows < half, np.cos(phase), np.where(rows == half, np.cos(nyquist), -np.sin(phase))
    )
    phase_back = (cols % half * rows % length).astype(np.float64) * step
    nyquist_back = (half * rows % length).astype(np.float64) * step
    weight = np.where(cols == 0, 1.0, 2.0)
    inverse = np.where(
        cols < half,
        weight * np.cos(phase_back),
        np.where(cols == half, np.cos(nyquist_back), -2.0 * np.sin(phase_back)),
    )
    return forward.astype(np.float32), (inverse / length).astype(np.float32)


def spectral_product(left, right, conjugate):
    half = left.shape[-1] // 2
    left_real, left_imag = (left[..., :half], left[..., half:])
    right_real, right_imag = (right[..., :half], right[..., half:])
    first_bin = lax.broadcasted_iota(jnp.int32, (1,) * (left.ndim - 1) + (half,), left.ndim - 1) == 0
    if conjugate:
        right_eff = jnp.where(first_bin, right_imag, -right_imag)
    else:
        right_eff = right_imag
    real_out = left_real * right_real - jnp.where(first_bin, 0.0, left_imag * right_eff)
    imag_out = jnp.where(
        first_bin, left_imag * right_imag, left_real * right_eff + left_imag * right_real
    )
    return jnp.concatenate([real_out, imag_out], axis=-1)


def rows_times(left, table):
    return lax.dot_general(
        left, table, (((left.ndim - 1,), (1,)), ((), ())),
        precision=HIGHEST_MODE, preferred_element_type=jnp.float32,
    )


def kdot(left, right):
    return jnp.dot(left, right, precision=lax.Precision.HIGH, preferred_element_type=jnp.float32)


def kdot_narrow(left, right):
    return jnp.dot(left, right, preferred_element_type=jnp.float32)


def split_taps(filt_spec, fr_ref, ff_ref, fm_ref):
    half = filt_spec.shape[1] // 2
    real, imag = filt_spec[:, :half], filt_spec[:, half:]
    first_bin = lax.broadcasted_iota(jnp.int32, real.shape, 1) == 0
    fr_ref[...] = real
    ff_ref[...] = jnp.where(first_bin, imag, real)
    fm_ref[...] = jnp.where(first_bin, 0.0, imag)


def block_terms(spec_ref, fr_ref, ff_ref, fm_ref, acc_ref, chans, pairs, conjugate):
    half = acc_ref.shape[1] // 2
    for out, terms in pairs:
        acc_real = jnp.zeros((chans, half), jnp.float32)
        acc_imag = jnp.zeros((chans, half), jnp.float32)
        for src, lag in terms:
            rows = pl.ds(src * chans, chans)
            taps = pl.ds(lag * chans, chans)
            left_real = spec_ref[rows, pl.ds(0, half)]
            left_imag = spec_ref[rows, pl.ds(half, half)]
            right_real = fr_ref[taps, :]
            right_first = ff_ref[taps, :]
            right_masked = fm_ref[taps, :]
            if conjugate:
                acc_real = acc_real + (left_real * right_real + left_imag * right_masked)
                acc_imag = acc_imag + (left_imag * right_first - left_real * right_masked)
            else:
                acc_real = acc_real + (left_real * right_real - left_imag * right_masked)
                acc_imag = acc_imag + (left_real * right_masked + left_imag * right_first)
        acc_ref[pl.ds(out * chans, chans), pl.ds(0, half)] = acc_real
        acc_ref[pl.ds(out * chans, chans), pl.ds(half, half)] = acc_imag


def forward_kernel(x_ref, fwd_ref, inv_ref, conv_ref, filt_ref, spec_ref, fr_ref, ff_ref, fm_ref, acc_ref):
    blocks, _, chans, tok = x_ref.shape
    rows = blocks * chans
    mixed = x_ref[:, 0, :, :].astype(jnp.float32).reshape(rows, tok)
    taps = x_ref[:, 1, :, :].astype(jnp.float32).reshape(rows, tok)
    table = fwd_ref[...]
    spec_ref[...] = kdot_narrow(mixed, table)
    filt_spec = kdot_narrow(taps, table)
    filt_ref[...] = filt_spec
    split_taps(filt_spec, fr_ref, ff_ref, fm_ref)
    pairs = [(out, [(out - lag, lag) for lag in range(out + 1)]) for out in range(blocks)]
    block_terms(spec_ref, fr_ref, ff_ref, fm_ref, acc_ref, chans, pairs, False)
    waveform = kdot(acc_ref[...], inv_ref[...])
    conv_ref[0:chans, :] = waveform[0:chans, :tok].astype(conv_ref.dtype)
    conv_ref[chans:, :] = (waveform[chans:, :tok] + waveform[: rows - chans, tok:]).astype(conv_ref.dtype)


def backward_kernel(chans, d_ref, filt_ref, fwd_ref, inv_ref, out_ref, fol_ref, spec_ref, fr_ref, ff_ref, fm_ref, acc_ref):
    rows, tok = d_ref.shape
    blocks = rows // chans
    dconv = d_ref[...].astype(jnp.float32)
    fol_ref[: rows - chans, :] = dconv[chans:, :]
    fol_ref[rows - chans :, :] = jnp.zeros((chans, tok), jnp.float32)
    spec_ref[...] = kdot_narrow(dconv, fwd_ref[:tok, :]) + kdot_narrow(fol_ref[...], fwd_ref[tok:, :])
    split_taps(filt_ref[...], fr_ref, ff_ref, fm_ref)
    pairs = [(out, [(out + lag, lag) for lag in range(blocks - out)]) for out in range(blocks)]
    block_terms(spec_ref, fr_ref, ff_ref, fm_ref, acc_ref, chans, pairs, True)
    out_ref[...] = kdot(acc_ref[...], inv_ref[...]).astype(out_ref.dtype)


def vmem_call(kernel, outs, scratch, *args):
    return pl.pallas_call(
        kernel,
        out_shape=outs,
        in_specs=[pl.BlockSpec(memory_space=pltpu.VMEM) for _ in args],
        out_specs=tuple(pl.BlockSpec(memory_space=pltpu.VMEM) for _ in outs),
        scratch_shapes=scratch,
    )(*args)


def to_channels(x, parts):
    tok, width = x.shape[-2], x.shape[-1]
    lead = x.shape[:-2]
    xt = jnp.swapaxes(x, -1, -2).reshape(lead + (parts, width // parts, tok))
    xt = jnp.moveaxis(xt, len(lead), 0)
    return lax.all_to_all(xt, "seq", 0, 0)


def from_channels(xc):
    back = lax.all_to_all(xc, "seq", 0, 0)
    back = jnp.moveaxis(back, 0, -3)
    shape = back.shape
    back = back.reshape(shape[:-3] + (shape[-3] * shape[-2], shape[-1]))
    return jnp.swapaxes(back, -1, -2)


def chan_sum(partial):
    count = lax.axis_size("chan")
    spread = jnp.broadcast_to(partial[None], (count,) + partial.shape)
    return jnp.sum(lax.all_to_all(spread, "chan", 0, 0), axis=0)


def body(stream_in, outer_gate, inner_gate, values, long_filter, norm_gain, cotangent):
    half = stream_in.shape[0]
    width = stream_in.shape[1]
    parts = lax.axis_size("seq")
    forward_np, inverse_np = dft_tables(half)

    inner = inner_gate.astype(jnp.float32)
    value_rows = values.astype(jnp.float32)
    eye = jnp.eye(width, dtype=jnp.bfloat16)

    def flipped(x):
        return lax.dot_general(eye, x, (((1,), (1,)), ((), ())), preferred_element_type=jnp.float32)

    stacked = jnp.stack(
        [flipped((inner * value_rows).astype(jnp.bfloat16)), flipped(long_filter)], axis=0
    ).astype(jnp.bfloat16)
    stacked = jnp.moveaxis(stacked.reshape(2, parts, width // parts, half), 1, 0)
    chan_in = lax.all_to_all(stacked, "seq", 0, 0)
    blocks, _, chans, tok = chan_in.shape
    rows = blocks * chans
    conv_c, filt_spec = vmem_call(
        forward_kernel,
        (
            jax.ShapeDtypeStruct((rows, tok), jnp.bfloat16),
            jax.ShapeDtypeStruct((rows, 2 * half), jnp.float32),
        ),
        [pltpu.VMEM((rows, 2 * half), jnp.float32)]
        + [pltpu.VMEM((rows, half), jnp.float32) for _ in range(3)]
        + [pltpu.VMEM((rows, 2 * half), jnp.float32)],
        chan_in, jnp.asarray(forward_np[:, :half].T), jnp.asarray(inverse_np.T),
    )
    conv_c = conv_c.reshape(blocks, chans, tok)
    conv = from_channels(conv_c).astype(jnp.float32)

    outer = outer_gate.astype(jnp.float32)
    resid = stream_in.astype(jnp.float32) + outer * conv
    scaled = cotangent.astype(jnp.float32) * norm_gain
    sums = chan_sum(
        jnp.concatenate(
            [
                jnp.sum(resid * resid, axis=1, keepdims=True),
                jnp.sum(scaled * resid, axis=1, keepdims=True),
            ],
            axis=1,
        )
    )
    square_sum, proj_sum = sums[:, 0:1], sums[:, 1:2]
    total_width = width * lax.axis_size("chan")
    inv_rms = lax.rsqrt(square_sum / total_width + EPSILON)
    normed = (resid * inv_rms * norm_gain).astype(jnp.bfloat16)
    grad_resid = inv_rms * (scaled - resid * inv_rms * inv_rms * (proj_sum / total_width))
    outer_grad = (grad_resid * conv).astype(jnp.bfloat16)
    dconv = grad_resid * outer

    dconv_c = to_channels(dconv.astype(jnp.bfloat16), parts).reshape(rows, tok)
    (dmixed_c,) = vmem_call(
        functools.partial(backward_kernel, chans),
        (jax.ShapeDtypeStruct((rows, tok), jnp.bfloat16),),
        [pltpu.VMEM((rows, tok), jnp.float32), pltpu.VMEM((rows, 2 * half), jnp.float32)]
        + [pltpu.VMEM((rows, half), jnp.float32) for _ in range(3)]
        + [pltpu.VMEM((rows, 2 * half), jnp.float32)],
        dconv_c, filt_spec, jnp.asarray(forward_np.T), jnp.asarray(inverse_np[:half].T),
    )
    dmixed_t = lax.all_to_all(dmixed_c.reshape(blocks, chans, tok), "seq", 0, 0).reshape(width, tok)
    dmixed = lax.dot_general(dmixed_t, eye, (((0,), (0,)), ((), ())), preferred_element_type=jnp.float32)
    inner_grad = (dmixed * value_rows).astype(jnp.bfloat16)
    value_grad = (dmixed * inner).astype(jnp.bfloat16)
    return (normed, grad_resid.astype(jnp.bfloat16), outer_grad, inner_grad, value_grad)


def solution(mesh):
    placed = (
        P("seq", "chan"),
        P("seq", "chan"),
        P("seq", "chan"),
        P("seq", "chan"),
        P("seq", "chan"),
        P("chan"),
        P("seq", "chan"),
    )
    return jax.shard_map(
        body,
        mesh=mesh,
        in_specs=placed,
        out_specs=(
            P("seq", "chan"),
            P("seq", "chan"),
            P("seq", "chan"),
            P("seq", "chan"),
            P("seq", "chan"),
        ),
        check_vma=False,
    )
```
